128 devices in a mesh: row: 16 (over x, z), col: 8 (over y, core).
Axes of the slice: x: 4, y: 4, z: 4, core: 2. Of those that a mesh axis runs over, the one named last changes fastest.
Arguments:
- front: float32 [16384, 16384], P('row', 'col')
- child_strips: float32 [16384, 32, 128], P(('row', 'col')), may hold values from -1.5 to 1.5
- child_owner: int32 [16384, 1], P(('row', 'col')), may hold values from 0 to 127; in each aligned block of 128 rows (0 to 127, 128 to 255, ...) at most 2 rows name the same one
- child_slot: int32 [16384], P(('row', 'col')), may hold values from 0 to 511
Outputs:
- factored: float32 [16384, 16384], P('row', 'col')
- panel: float32 [16384, 512], P('row')
The draws below stay inside these ranges and needn't reach their ends.
Inputs may be any that keep to these rules, and one draw needn't show every extreme that they name: `child_owner`: among the rows of one device (aligned blocks of 128 rows), no owner is named more than 2 times.
All inputs are finite; a program needn't handle non-finite values.
Results may differ from the reference program's by a relative error of at most 0.00008.
Values sent between devices are 32-bit elements; how exact they have to be, the bound alone decides.
No kernel may reach another device: no remote copies, remote signals or barrier semaphores. Data moves between devices by JAX's collectives and lax.ppermute only.
A program may use at most 128 MiB of HBM per device.

```python
import math
import jax
import jax.numpy as jnp
import numpy as np
from jax import lax

FRONT = 16384
PANEL = 512
STRIP_ROWS = 32
STRIP_COLS = 128
CHILD_DEV = 128
CAPACITY = 2
CHILD = 16384
LOCAL_STRIPS = 512
N_ROW = 16
N_COL = 8
DEVICES = 128


def draw_front(key, part):
    offdiag = 0.25 * jax.random.normal(key, (FRONT, FRONT), jnp.float32)
    offdiag = 0.7071 * (offdiag + offdiag.T)
    rows_idx = lax.broadcasted_iota(jnp.int32, (FRONT, FRONT), 0)
    cols_idx = lax.broadcasted_iota(jnp.int32, (FRONT, FRONT), 1)
    return jnp.where(rows_idx == cols_idx, 28.0 + offdiag, offdiag).astype(jnp.float32)


def place_ends(result, own_key, low, top_value):
    longest = result.shape.index(max(result.shape))
    spots = []
    for shift in (0, 1):
        where = [jax.random.randint(jax.random.fold_in(own_key, axis), (), 0, length) for axis, length in enumerate(result.shape)]
        where[longest] = (where[longest] + shift) % result.shape[longest]
        spots.append(tuple(where))
    return result.at[spots[0]].set(low).at[spots[1]].set(top_value)


def shard_levels(rng, shape, shards, least, top_value):
    def one(dim, blocks):
        draws = jax.random.uniform(jax.random.fold_in(jax.random.fold_in(rng, 6), dim), (blocks,), jnp.float32, least / len(shards), top_value / len(shards))
        return jnp.repeat(jnp.exp(draws), shape[dim] // blocks).reshape((-1,) + (1,) * (len(shape) - dim - 1))

    level = one(*shards[0])
    for cut in shards[1:]:
        level = level * one(*cut)
    return level


def shared_out(stream_key, own, number, rows, number_of, top, reach, skew):
    sequence = jax.random.permutation(stream_key, number_of)
    crowded, ordinary = portions_of(number_of, rows * top, reach, skew, True), portions_of(number_of, rows * top, reach, skew, False)
    places = jnp.arange(number_of)

    def named(sizes, rotation):
        used = int((sizes > 0).sum())
        fixed = max(1, used // 4)
        passed = fixed + (places - fixed + rotation * (used - fixed)) % max(1, number_of - fixed)
        return jnp.zeros((number_of,), jnp.int32).at[sequence[jnp.where(places < fixed, places, passed)]].set(jnp.asarray(sizes, jnp.int32))

    sizes = jnp.where(number % 4 == 0, named(crowded, number // 4), named(ordinary, number - number // 4 - 1))
    mixed = jax.random.permutation(jax.random.fold_in(own, 3), number_of)
    donor, sink = mixed[0:number_of // 2 * 2:2], mixed[1:number_of // 2 * 2:2]
    room = jnp.minimum(sizes[donor] - 1, reach - sizes[sink]) // 2
    room = jnp.where((donor == sequence[0]) | (sink == sequence[0]) | (sizes[sink] == 0), 0, jnp.maximum(room, 0))
    passed = jax.random.randint(jax.random.fold_in(own, 4), (number_of // 2,), 0, 1 << 20) % (room + 1)
    sizes = sizes.at[donor].add(-passed).at[sink].add(passed)
    items = jnp.searchsorted(jnp.cumsum(sizes), jnp.arange(rows * top), side="right").astype(jnp.int32)
    grid = items.reshape(top, rows).T
    grid = grid[jax.random.permutation(jax.random.fold_in(own, 1), rows)]
    rotation = jax.random.randint(jax.random.fold_in(own, 2), (rows, 1), 0, top)
    return jnp.take_along_axis(grid, (jnp.arange(top)[None, :] + rotation) % top, axis=1)


def portions_of(number_of, total, reach, lean, full):
    loads = [(1 << 20) // math.isqrt(grade ** lean) + 1 for grade in range(1, number_of + 1)]
    largest = reach if full else min(reach, max(-(-total // number_of), total * loads[0] // sum(loads)))
    least = 1 if total - largest >= number_of - 1 else 0
    holding, surplus = [largest] + [least] * (number_of - 1), total - largest - least * (number_of - 1)
    while surplus > 0:
        candidates = [i for i in range(1, number_of) if holding[i] < largest] or [i for i in range(1, number_of) if holding[i] < reach]
        mass, remaining = sum([loads[i] for i in candidates]), surplus
        for i in candidates:
            more = min(reach - holding[i], max(1, remaining * loads[i] // mass), surplus)
            holding[i] = holding[i] + more
            surplus = surplus - more
    return np.array(holding)


def bell_draw(rng, extent, scale, limit, cuts=(), dtype=jnp.bfloat16):
    gain = shard_levels(rng, extent, cuts, -0.22, 0.18) if cuts else 1.0
    entries = jax.random.normal(rng, extent, jnp.float32) * scale * gain
    return jnp.minimum(jnp.maximum(entries, -limit), limit).astype(dtype)


def setup_inputs(seed: int = 0) -> dict:
    seeds = jax.random.split(jax.random.key(seed), 5)
    front = draw_front(jax.random.fold_in(seeds[4], 71), 0)
    child_strips = bell_draw(seeds[1], (CHILD, STRIP_ROWS, STRIP_COLS), 0.25, 1.5, ((0, 128),), jnp.float32)
    child_owner_keys = jax.random.split(jax.random.fold_in(seeds[2], 1), CHILD // CHILD_DEV)
    child_owner_turns = jax.random.permutation(jax.random.fold_in(seeds[2], 3), CHILD // CHILD_DEV)
    child_owner = jax.vmap(lambda own, number: shared_out(jax.random.fold_in(seeds[2], 2), own, number, CHILD_DEV, DEVICES, 1, CAPACITY, 2))(child_owner_keys, child_owner_turns).reshape((CHILD, 1))
    child_slot = place_ends(jax.random.randint(seeds[3], (CHILD,), 0, LOCAL_STRIPS), jax.random.fold_in(seeds[3], 1), 0, LOCAL_STRIPS - 1).astype(jnp.int32)
    return dict(front=front, child_strips=child_strips, child_owner=child_owner, child_slot=child_slot)


def reference(front, child_strips, child_owner, child_slot):
    rows_dev = FRONT // N_ROW
    cols_dev = FRONT // N_COL
    strips_across = cols_dev // STRIP_COLS
    strips_down = rows_dev // STRIP_ROWS
    owner = child_owner[:, 0]
    grow = owner // N_COL * strips_down + child_slot // strips_across
    gcol = owner % N_COL * strips_across + child_slot % strips_across
    tiles = front.reshape(FRONT // STRIP_ROWS, STRIP_ROWS, FRONT // STRIP_COLS, STRIP_COLS)
    tiles = tiles.at[grow.astype(jnp.int32), :, gcol.astype(jnp.int32), :].add(child_strips)
    assembled = tiles.reshape(FRONT, FRONT)
    block = assembled[:PANEL, :PANEL]
    factor11 = jnp.linalg.cholesky(0.5 * (block + block.T))
    below = assembled[PANEL:, :PANEL]
    solved = lax.linalg.triangular_solve(factor11, below, left_side=False, lower=True, transpose_a=True)
    panel = jnp.concatenate([factor11, solved], axis=0)
    update = jnp.dot(solved.astype(jnp.float32), solved.T.astype(jnp.float32), preferred_element_type=jnp.float32, precision=lax.Precision.HIGHEST)
    factored = assembled.at[PANEL:, PANEL:].add(-update)
    return (factored, panel)
```

```python
import jax
import jax.numpy as jnp
from jax import lax
from jax.sharding import PartitionSpec as P

PANEL = 512


def top_block_part(child_strips, owner, child_slot, strips_across):
    strip_r = child_strips.shape[1]
    strip_c = child_strips.shape[2]
    down = PANEL // strip_r
    across = PANEL // strip_c
    srow = child_slot // strips_across
    scol = child_slot % strips_across
    hit = (owner == 0) & (srow < down) & (scol < across)
    where = jnp.where(hit, srow * across + scol, down * across)
    part = jnp.zeros((down * across, strip_r, strip_c), jnp.float32)
    part = part.at[where].add(child_strips, mode="drop")
    part = part.reshape(down, across, strip_r, strip_c).transpose(0, 2, 1, 3)
    return part.reshape(PANEL, PANEL)


def shards(front, child_strips, child_owner, child_slot):
    row_count = lax.axis_size("row")
    col_count = lax.axis_size("col")
    devices = row_count * col_count
    rows_dev, cols_dev = front.shape
    strip_r = child_strips.shape[1]
    strip_c = child_strips.shape[2]
    held = child_strips.shape[0]
    capacity = max(2, 2 * held // devices)
    strips_down = rows_dev // strip_r
    strips_across = cols_dev // strip_c
    local_count = strips_down * strips_across
    owner = child_owner[:, 0]
    row_id = lax.axis_index("row")
    col_id = lax.axis_index("col")
    is_owner = (row_id == 0) & (col_id == 0)

    part = top_block_part(child_strips, owner, child_slot, strips_across)
    part = part + jnp.where(is_owner, front[:PANEL, :PANEL], 0.0)
    top_block = lax.psum(part, ("row", "col"))
    factor11 = jnp.linalg.cholesky(0.5 * (top_block + top_block.T))

    positions = jnp.arange(held, dtype=jnp.int32)
    same_owner = owner[:, None] == owner[None, :]
    earlier = positions[:, None] > positions[None, :]
    rank = jnp.sum((same_owner & earlier).astype(jnp.int32), axis=1)
    target = owner * capacity + rank
    outgoing = (
        jnp.zeros((devices * capacity, strip_r, strip_c), jnp.float32).at[target].set(child_strips)
    )
    places = jnp.full((devices * capacity,), local_count, jnp.int32).at[target].set(child_slot)
    arrived, landing = (
        lax.all_to_all(
            outgoing.reshape(devices, capacity, strip_r, strip_c),
            ("row", "col"),
            split_axis=0,
            concat_axis=0,
            tiled=True,
        ),
        lax.all_to_all(
            places.reshape(devices, capacity),
            ("row", "col"),
            split_axis=0,
            concat_axis=0,
            tiled=True,
        ),
    )
    arrived = arrived.reshape(devices * capacity, strip_r, strip_c)
    landing = landing.reshape(devices * capacity)
    tiles = front.reshape(strips_down, strip_r, strips_across, strip_c)
    tiles = tiles.at[landing // strips_across, :, landing % strips_across, :].add(
        arrived, mode="drop"
    )
    assembled = tiles.reshape(rows_dev, cols_dev)

    raw = jnp.where(col_id == 0, assembled[:, :PANEL], 0.0)
    piece = lax.psum_scatter(raw, "col", scatter_dimension=0, tiled=True)
    piece_rows = piece.shape[0]
    solved = lax.linalg.triangular_solve(
        factor11, piece, left_side=False, lower=True, transpose_a=True
    )
    first = row_id * rows_dev + col_id * piece_rows
    head = lax.dynamic_slice_in_dim(factor11, jnp.minimum(first, PANEL - piece_rows), piece_rows, 0)
    solved = jnp.where(first < PANEL, head, solved)
    panel_here = lax.all_gather(solved, "col", axis=0, tiled=True)

    ratio = row_count // col_count
    got = []
    for o in range(ratio):
        perm = []
        for k in range(row_count):
            c, b = divmod(k, ratio)
            for j in range(col_count):
                perm.append((k * col_count + j, (ratio * j + (b + o) % ratio) * col_count + c))
        got.append(lax.ppermute(panel_here, ("row", "col"), perm))
    t = row_id % ratio
    pieces = []
    for b in range(ratio):
        pick = got[0]
        for o in range(ratio):
            pick = jnp.where((b + o) % ratio == t, got[o], pick)
        pieces.append(pick)
    column_panel = jnp.concatenate(pieces, axis=0)
    update = lax.dot_general(
        panel_here,
        column_panel,
        (((1,), (1,)), ((), ())),
        precision=lax.Precision.HIGHEST,
        preferred_element_type=jnp.float32,
    )
    global_rows = row_id * rows_dev + jnp.arange(rows_dev, dtype=jnp.int32)
    global_cols = col_id * cols_dev + jnp.arange(cols_dev, dtype=jnp.int32)
    trailing = (global_rows[:, None] >= PANEL) & (global_cols[None, :] >= PANEL)
    factored = assembled - jnp.where(trailing, update, 0.0)
    return (factored, panel_here)


def solution(mesh):
    in_specs = (
        P("row", "col"),
        P(("row", "col"), None, None),
        P(("row", "col"), None),
        P(("row", "col")),
    )
    out_specs = (P("row", "col"), P("row", None))
    return jax.shard_map(shards, mesh=mesh, in_specs=in_specs, out_specs=out_specs, check_vma=False)
```

```python
import jax
import jax.numpy as jnp
from jax import lax
from jax.sharding import PartitionSpec as P

PANEL = 512


def spread(value, axis, source):
    kept = jnp.where(lax.axis_index(axis) == source, value, 0).astype(value.dtype)
    return lax.psum(kept, axis)


def shards(front, child_strips, child_owner, child_slot):
    row_count = lax.axis_size("row")
    col_count = lax.axis_size("col")
    devices = row_count * col_count
    rows_dev, cols_dev = front.shape
    strip_r = child_strips.shape[1]
    strip_c = child_strips.shape[2]
    held = child_strips.shape[0]
    capacity = max(2, 2 * held // devices)
    strips_down = rows_dev // strip_r
    strips_across = cols_dev // strip_c
    local_count = strips_down * strips_across
    owner = child_owner[:, 0]
    positions = jnp.arange(held, dtype=jnp.int32)
    same_owner = owner[:, None] == owner[None, :]
    earlier = positions[:, None] > positions[None, :]
    rank = jnp.sum((same_owner & earlier).astype(jnp.int32), axis=1)
    target = owner * capacity + rank
    outgoing = (
        jnp.zeros((devices * capacity, strip_r, strip_c), jnp.float32).at[target].set(child_strips)
    )
    places = jnp.full((devices * capacity,), local_count, jnp.int32).at[target].set(child_slot)
    arrived, landing = (
        lax.all_to_all(
            outgoing.reshape(devices, capacity, strip_r, strip_c),
            ("row", "col"),
            split_axis=0,
            concat_axis=0,
            tiled=True,
        ),
        lax.all_to_all(
            places.reshape(devices, capacity),
            ("row", "col"),
            split_axis=0,
            concat_axis=0,
            tiled=True,
        ),
    )
    arrived = arrived.reshape(devices * capacity, strip_r, strip_c)
    landing = landing.reshape(devices * capacity)
    row_id = lax.axis_index("row")
    col_id = lax.axis_index("col")
    first_rows = row_id == 0
    is_owner = first_rows & (col_id == 0)

    down = PANEL // strip_r
    across = PANEL // strip_c
    srow = landing // strips_across
    scol = landing % strips_across
    hit = (srow < down) & (scol < across)
    spot = jnp.where(hit, srow * across + scol, down * across)
    part = jnp.zeros((down * across, strip_r, strip_c), jnp.float32)
    part = part.at[spot].add(arrived, mode="drop")
    part = part.reshape(down, across, strip_r, strip_c).transpose(0, 2, 1, 3).reshape(PANEL, PANEL)
    top_block = front[:PANEL, :PANEL] + part
    safe_block = jnp.where(
        is_owner, 0.5 * (top_block + top_block.T), jnp.eye(PANEL, dtype=jnp.float32)
    )
    factor11 = jnp.linalg.cholesky(safe_block)

    pieces_l = factor11.reshape(row_count, PANEL // row_count, PANEL)
    held_l = jnp.where(first_rows, pieces_l[0], 0.0)
    for r in range(1, row_count):
        got = lax.ppermute(pieces_l[r], ("row", "col"), [(0, r * col_count)])
        held_l = held_l + got
    factor_col0 = lax.all_gather(held_l, "row", axis=0, tiled=True)

    tiles = front.reshape(strips_down, strip_r, strips_across, strip_c)
    tiles = tiles.at[landing // strips_across, :, landing % strips_across, :].add(
        arrived, mode="drop"
    )
    assembled = tiles.reshape(rows_dev, cols_dev)

    solved = lax.linalg.triangular_solve(
        factor_col0, assembled[:, :PANEL], left_side=False, lower=True, transpose_a=True
    )
    headed = jnp.concatenate([factor_col0, solved[PANEL:]], axis=0)
    solved = jnp.where(first_rows, headed, solved)
    panel_here = spread(solved, "col", 0)

    ratio = row_count // col_count
    piece_rows = rows_dev // col_count
    mine = None
    for j in range(col_count):
        perm = []
        for k in range(row_count):
            c, b = divmod(k, ratio)
            perm.append((k * col_count, (col_count * b + j) * col_count + c))
        got = lax.ppermute(solved[j * piece_rows:(j + 1) * piece_rows], ("row", "col"), perm)
        mine = got if mine is None else jnp.where(row_id % col_count == j, got, mine)
    column_panel = lax.all_gather(mine, "row", axis=0, tiled=True)
    update = lax.dot_general(
        panel_here,
        column_panel,
        (((1,), (1,)), ((), ())),
        precision=lax.Precision.HIGHEST,
        preferred_element_type=jnp.float32,
    )
    global_rows = row_id * rows_dev + jnp.arange(rows_dev, dtype=jnp.int32)
    global_cols = col_id * cols_dev + jnp.arange(cols_dev, dtype=jnp.int32)
    trailing = (global_rows[:, None] >= PANEL) & (global_cols[None, :] >= PANEL)
    factored = assembled - jnp.where(trailing, update, 0.0)
    return (factored, panel_here)


def solution(mesh):
    in_specs = (
        P("row", "col"),
        P(("row", "col"), None, None),
        P(("row", "col"), None),
        P(("row", "col")),
    )
    out_specs = (P("row", "col"), P("row", None))
    return jax.shard_map(shards, mesh=mesh, in_specs=in_specs, out_specs=out_specs, check_vma=False)
```

```python
import jax
import jax.numpy as jnp
from jax import lax
from jax.sharding import PartitionSpec as P

PANEL = 512


def shards(front, child_strips, child_owner, child_slot):
    row_count = lax.axis_size("row")
    col_count = lax.axis_size("col")
    devices = row_count * col_count
    rows_dev, cols_dev = front.shape
    strip_r = child_strips.shape[1]
    strip_c = child_strips.shape[2]
    held = child_strips.shape[0]
    capacity = max(2, 2 * held // devices)
    strips_down = rows_dev // strip_r
    strips_across = cols_dev // strip_c
    local_count = strips_down * strips_across
    owner = child_owner[:, 0]
    positions = jnp.arange(held, dtype=jnp.int32)
    same_owner = owner[:, None] == owner[None, :]
    earlier = positions[:, None] > positions[None, :]
    rank = jnp.sum((same_owner & earlier).astype(jnp.int32), axis=1)
    target = owner * capacity + rank
    outgoing = (
        jnp.zeros((devices * capacity, strip_r, strip_c), jnp.float32).at[target].set(child_strips)
    )
    places = jnp.full((devices * capacity,), local_count, jnp.int32).at[target].set(child_slot)
    arrived, landing = (
        lax.all_to_all(
            outgoing.reshape(devices, capacity, strip_r, strip_c),
            ("row", "col"),
            split_axis=0,
            concat_axis=0,
            tiled=True,
        ),
        lax.all_to_all(
            places.reshape(devices, capacity),
            ("row", "col"),
            split_axis=0,
            concat_axis=0,
            tiled=True,
        ),
    )
    arrived = arrived.reshape(devices * capacity, strip_r, strip_c)
    landing = landing.reshape(devices * capacity)
    row_id = lax.axis_index("row")
    col_id = lax.axis_index("col")
    first_rows = row_id == 0
    is_owner = first_rows & (col_id == 0)

    down = PANEL // strip_r
    across = PANEL // strip_c
    srow = landing // strips_across
    scol = landing % strips_across
    hit = (srow < down) & (scol < across)
    spot = jnp.where(hit, srow * across + scol, down * across)
    pick = (spot[None, :] == jnp.arange(down * across, dtype=jnp.int32)[:, None]).astype(jnp.float32)
    part = lax.dot_general(
        pick,
        arrived.reshape(arrived.shape[0], strip_r * strip_c),
        (((1,), (0,)), ((), ())),
        precision=lax.Precision.HIGHEST,
        preferred_element_type=jnp.float32,
    )
    part = part.reshape(down, across, strip_r, strip_c).transpose(0, 2, 1, 3).reshape(PANEL, PANEL)
    top_block = front[:PANEL, :PANEL] + part
    safe_block = jnp.where(
        is_owner, 0.5 * (top_block + top_block.T), jnp.eye(PANEL, dtype=jnp.float32)
    )
    factor11 = jnp.linalg.cholesky(safe_block)

    pieces_l = factor11.reshape(row_count, PANEL // row_count, PANEL)
    held_l = jnp.where(first_rows, pieces_l[0], 0.0)
    for r in range(1, row_count):
        got = lax.ppermute(pieces_l[r], ("row", "col"), [(0, r * col_count)])
        held_l = held_l + got
    factor_col0 = lax.all_gather(held_l, "row", axis=0, tiled=True)

    tiles = front.reshape(strips_down, strip_r, strips_across, strip_c)
    tiles = tiles.at[landing // strips_across, :, landing % strips_across, :].add(
        arrived, mode="drop"
    )
    assembled = tiles.reshape(rows_dev, cols_dev)

    solved = lax.linalg.triangular_solve(
        factor_col0, assembled[:, :PANEL], left_side=False, lower=True, transpose_a=True
    )
    headed = jnp.concatenate([factor_col0, solved[PANEL:]], axis=0)
    solved = jnp.where(first_rows, headed, solved)
    piece_rows = rows_dev // col_count
    my_piece = solved[:piece_rows]
    for j in range(1, col_count):
        perm = [(k * col_count, k * col_count + j) for k in range(row_count)]
        got = lax.ppermute(solved[j * piece_rows:(j + 1) * piece_rows], ("row", "col"), perm)
        my_piece = jnp.where(col_id == j, got, my_piece)

    ratio = row_count // col_count
    perm = []
    for k in range(row_count):
        c, b = divmod(k, ratio)
        for j in range(col_count):
            perm.append((k * col_count + j, (col_count * b + j) * col_count + c))
    mine = lax.ppermute(my_piece, ("row", "col"), perm)
    column_panel = lax.all_gather(mine, "row", axis=0, tiled=True)
    panel_here = lax.all_gather(my_piece, "col", axis=0, tiled=True)
    update = lax.dot_general(
        panel_here,
        column_panel,
        (((1,), (1,)), ((), ())),
        precision=lax.Precision.HIGHEST,
        preferred_element_type=jnp.float32,
    )
    global_rows = row_id * rows_dev + jnp.arange(rows_dev, dtype=jnp.int32)
    global_cols = col_id * cols_dev + jnp.arange(cols_dev, dtype=jnp.int32)
    trailing = (global_rows[:, None] >= PANEL) & (global_cols[None, :] >= PANEL)
    factored = assembled - jnp.where(trailing, update, 0.0)
    return (factored, panel_here)


def solution(mesh):
    in_specs = (
        P("row", "col"),
        P(("row", "col"), None, None),
        P(("row", "col"), None),
        P(("row", "col")),
    )
    out_specs = (P("row", "col"), P("row", None))
    return jax.shard_map(shards, mesh=mesh, in_specs=in_specs, out_specs=out_specs, check_vma=False)
```

```python
import jax
import jax.numpy as jnp
from jax import lax
from jax.sharding import PartitionSpec as P

PANEL = 512


def shards(front, child_strips, child_owner, child_slot):
    row_count = lax.axis_size("row")
    col_count = lax.axis_size("col")
    devices = row_count * col_count
    rows_dev, cols_dev = front.shape
    strip_r = child_strips.shape[1]
    strip_c = child_strips.shape[2]
    held = child_strips.shape[0]
    capacity = max(2, 2 * held // devices)
    strips_down = rows_dev // strip_r
    strips_across = cols_dev // strip_c
    local_count = strips_down * strips_across
    owner = child_owner[:, 0]
    positions = jnp.arange(held, dtype=jnp.int32)
    same_owner = owner[:, None] == owner[None, :]
    earlier = positions[:, None] > positions[None, :]
    rank = jnp.sum((same_owner & earlier).astype(jnp.int32), axis=1)
    target = owner * capacity + rank
    route = (target[None, :] == jnp.arange(devices * capacity, dtype=jnp.int32)[:, None]).astype(jnp.float32)
    outgoing = lax.dot_general(
        route,
        child_strips.reshape(held, strip_r * strip_c),
        (((1,), (0,)), ((), ())),
        precision=lax.Precision.HIGHEST,
        preferred_element_type=jnp.float32,
    )
    places = jnp.full((devices * capacity,), local_count, jnp.int32).at[target].set(child_slot)
    arrived, landing = (
        lax.all_to_all(
            outgoing.reshape(devices, capacity, strip_r, strip_c),
            ("row", "col"),
            split_axis=0,
            concat_axis=0,
            tiled=True,
        ),
        lax.all_to_all(
            places.reshape(devices, capacity),
            ("row", "col"),
            split_axis=0,
            concat_axis=0,
            tiled=True,
        ),
    )
    arrived = arrived.reshape(devices * capacity, strip_r, strip_c)
    landing = landing.reshape(devices * capacity)
    row_id = lax.axis_index("row")
    col_id = lax.axis_index("col")
    first_rows = row_id == 0
    is_owner = first_rows & (col_id == 0)

    down = PANEL // strip_r
    across = PANEL // strip_c
    srow = landing // strips_across
    scol = landing % strips_across
    hit = (srow < down) & (scol < across)
    spot = jnp.where(hit, srow * across + scol, down * across)
    pick = (spot[None, :] == jnp.arange(down * across, dtype=jnp.int32)[:, None]).astype(jnp.float32)
    part = lax.dot_general(
        pick,
        arrived.reshape(arrived.shape[0], strip_r * strip_c),
        (((1,), (0,)), ((), ())),
        precision=lax.Precision.HIGHEST,
        preferred_element_type=jnp.float32,
    )
    part = part.reshape(down, across, strip_r, strip_c).transpose(0, 2, 1, 3).reshape(PANEL, PANEL)
    top_block = front[:PANEL, :PANEL] + part
    safe_block = jnp.where(
        is_owner, 0.5 * (top_block + top_block.T), jnp.eye(PANEL, dtype=jnp.float32)
    )
    factor11 = jnp.linalg.cholesky(safe_block)

    pieces_l = factor11.reshape(row_count, PANEL // row_count, PANEL)
    held_l = jnp.where(first_rows, pieces_l[0], 0.0)
    for r in range(1, row_count):
        got = lax.ppermute(pieces_l[r], ("row", "col"), [(0, r * col_count)])
        held_l = held_l + got
    factor_col0 = lax.all_gather(held_l, "row", axis=0, tiled=True)

    tiles = front.reshape(strips_down, strip_r, strips_across, strip_c)
    tiles = tiles.at[landing // strips_across, :, landing % strips_across, :].add(
        arrived, mode="drop"
    )
    assembled = tiles.reshape(rows_dev, cols_dev)

    solved = lax.linalg.triangular_solve(
        factor_col0, assembled[:, :PANEL], left_side=False, lower=True, transpose_a=True
    )
    headed = jnp.concatenate([factor_col0, solved[PANEL:]], axis=0)
    solved = jnp.where(first_rows, headed, solved)
    piece_rows = rows_dev // col_count
    my_piece = solved[:piece_rows]
    for j in range(1, col_count):
        perm = [(k * col_count, k * col_count + j) for k in range(row_count)]
        got = lax.ppermute(solved[j * piece_rows:(j + 1) * piece_rows], ("row", "col"), perm)
        my_piece = jnp.where(col_id == j, got, my_piece)

    ratio = row_count // col_count
    perm = []
    for k in range(row_count):
        c, b = divmod(k, ratio)
        for j in range(col_count):
            perm.append((k * col_count + j, (col_count * b + j) * col_count + c))
    mine = lax.ppermute(my_piece, ("row", "col"), perm)
    column_panel = lax.all_gather(mine, "row", axis=0, tiled=True)
    shifted = [my_piece]
    for s_ in range(1, col_count):
        perm = [
            (k * col_count + j, k * col_count + (j + s_) % col_count)
            for k in range(row_count)
            for j in range(col_count)
        ]
        shifted.append(lax.ppermute(my_piece, ("row", "col"), perm))
    turned = jnp.stack([shifted[(col_count - m) % col_count] for m in range(col_count)] * 2)
    panel_here = lax.dynamic_slice_in_dim(turned, (col_count - col_id) % col_count, col_count, 0)
    panel_here = panel_here.reshape(rows_dev, PANEL)
    update = lax.dot_general(
        panel_here,
        column_panel,
        (((1,), (1,)), ((), ())),
        precision=lax.Precision.HIGHEST,
        preferred_element_type=jnp.float32,
    )
    global_rows = row_id * rows_dev + jnp.arange(rows_dev, dtype=jnp.int32)
    global_cols = col_id * cols_dev + jnp.arange(cols_dev, dtype=jnp.int32)
    trailing = (global_rows[:, None] >= PANEL) & (global_cols[None, :] >= PANEL)
    factored = assembled - jnp.where(trailing, update, 0.0)
    return (factored, panel_here)


def solution(mesh):
    in_specs = (
        P("row", "col"),
        P(("row", "col"), None, None),
        P(("row", "col"), None),
        P(("row", "col")),
    )
    out_specs = (P("row", "col"), P("row", None))
    return jax.shard_map(shards, mesh=mesh, in_specs=in_specs, out_specs=out_specs, check_vma=False)
```

```python
import jax
import jax.numpy as jnp
from jax import lax
from jax.sharding import PartitionSpec as P

PANEL = 512


def shards(front, child_strips, child_owner, child_slot):
    row_count = lax.axis_size("row")
    col_count = lax.axis_size("col")
    devices = row_count * col_count
    rows_dev, cols_dev = front.shape
    strip_r = child_strips.shape[1]
    strip_c = child_strips.shape[2]
    held = child_strips.shape[0]
    capacity = max(2, 2 * held // devices)
    strips_down = rows_dev // strip_r
    strips_across = cols_dev // strip_c
    local_count = strips_down * strips_across
    owner = child_owner[:, 0]
    positions = jnp.arange(held, dtype=jnp.int32)
    same_owner = owner[:, None] == owner[None, :]
    earlier = positions[:, None] > positions[None, :]
    rank = jnp.sum((same_owner & earlier).astype(jnp.int32), axis=1)
    target = owner * capacity + rank
    route = (target[None, :] == jnp.arange(devices * capacity, dtype=jnp.int32)[:, None]).astype(jnp.float32)
    outgoing = lax.dot_general(
        route,
        child_strips.reshape(held, strip_r * strip_c),
        (((1,), (0,)), ((), ())),
        precision=lax.Precision.HIGHEST,
        preferred_element_type=jnp.float32,
    )
    places = jnp.full((devices * capacity,), local_count, jnp.int32).at[target].set(child_slot)
    arrived, landing = (
        lax.all_to_all(
            outgoing.reshape(devices, capacity, strip_r, strip_c),
            ("row", "col"),
            split_axis=0,
            concat_axis=0,
            tiled=True,
        ),
        lax.all_to_all(
            places.reshape(devices, capacity),
            ("row", "col"),
            split_axis=0,
            concat_axis=0,
            tiled=True,
        ),
    )
    arrived = arrived.reshape(devices * capacity, strip_r, strip_c)
    landing = landing.reshape(devices * capacity)
    row_id = lax.axis_index("row")
    col_id = lax.axis_index("col")
    first_rows = row_id == 0
    is_owner = first_rows & (col_id == 0)

    across = PANEL // strip_c
    srow = landing // strips_across
    scol = landing % strips_across
    hit = (srow < strips_down) & (scol < across)
    spot = jnp.where(hit, srow * across + scol, strips_down * across)
    pick = (spot[None, :] == jnp.arange(strips_down * across, dtype=jnp.int32)[:, None]).astype(jnp.float32)
    part = lax.dot_general(
        pick,
        arrived.reshape(arrived.shape[0], strip_r * strip_c),
        (((1,), (0,)), ((), ())),
        precision=lax.Precision.HIGHEST,
        preferred_element_type=jnp.float32,
    )
    part = part.reshape(strips_down, across, strip_r, strip_c).transpose(0, 2, 1, 3)
    panel_cols = front[:, :PANEL] + part.reshape(rows_dev, PANEL)
    top_block = panel_cols[:PANEL]
    safe_block = jnp.where(
        is_owner, 0.5 * (top_block + top_block.T), jnp.eye(PANEL, dtype=jnp.float32)
    )
    factor11 = jnp.linalg.cholesky(safe_block)

    pieces_l = factor11.reshape(row_count, PANEL // row_count, PANEL)
    held_l = jnp.where(first_rows, pieces_l[0], 0.0)
    for r in range(1, row_count):
        got = lax.ppermute(pieces_l[r], ("row", "col"), [(0, r * col_count)])
        held_l = held_l + got
    factor_col0 = lax.all_gather(held_l, "row", axis=0, tiled=True)

    tiles = front.reshape(strips_down, strip_r, strips_across, strip_c)
    tiles = tiles.at[landing // strips_across, :, landing % strips_across, :].add(
        arrived, mode="drop"
    )
    assembled = tiles.reshape(rows_dev, cols_dev)

    solved = lax.linalg.triangular_solve(
        factor_col0, panel_cols, left_side=False, lower=True, transpose_a=True
    )
    headed = jnp.concatenate([factor_col0, solved[PANEL:]], axis=0)
    solved = jnp.where(first_rows, headed, solved)
    piece_rows = rows_dev // col_count
    my_piece = solved[:piece_rows]
    for j in range(1, col_count):
        perm = [(k * col_count, k * col_count + j) for k in range(row_count)]
        got = lax.ppermute(solved[j * piece_rows:(j + 1) * piece_rows], ("row", "col"), perm)
        my_piece = jnp.where(col_id == j, got, my_piece)

    ratio = row_count // col_count
    perm = []
    for k in range(row_count):
        c, b = divmod(k, ratio)
        for j in range(col_count):
            perm.append((k * col_count + j, (col_count * b + j) * col_count + c))
    mine = lax.ppermute(my_piece, ("row", "col"), perm)
    column_panel = lax.all_gather(mine, "row", axis=0, tiled=True)
    shifted = [my_piece]
    for s_ in range(1, col_count):
        perm = [
            (k * col_count + j, k * col_count + (j + s_) % col_count)
            for k in range(row_count)
            for j in range(col_count)
        ]
        shifted.append(lax.ppermute(my_piece, ("row", "col"), perm))
    turned = jnp.stack([shifted[(col_count - m) % col_count] for m in range(col_count)] * 2)
    panel_here = lax.dynamic_slice_in_dim(turned, (col_count - col_id) % col_count, col_count, 0)
    panel_here = panel_here.reshape(rows_dev, PANEL)
    update = lax.dot_general(
        panel_here,
        column_panel,
        (((1,), (1,)), ((), ())),
        precision=lax.Precision.HIGH,
        preferred_element_type=jnp.float32,
    )
    global_rows = row_id * rows_dev + jnp.arange(rows_dev, dtype=jnp.int32)
    global_cols = col_id * cols_dev + jnp.arange(cols_dev, dtype=jnp.int32)
    trailing = (global_rows[:, None] >= PANEL) & (global_cols[None, :] >= PANEL)
    factored = assembled - jnp.where(trailing, update, 0.0)
    return (factored, panel_here)


def solution(mesh):
    in_specs = (
        P("row", "col"),
        P(("row", "col"), None, None),
        P(("row", "col"), None),
        P(("row", "col")),
    )
    out_specs = (P("row", "col"), P("row", None))
    return jax.shard_map(shards, mesh=mesh, in_specs=in_specs, out_specs=out_specs, check_vma=False)
```

```python
import jax
import jax.numpy as jnp
from jax import lax
from jax.sharding import PartitionSpec as P

PANEL = 512


def shards(front, child_strips, child_owner, child_slot):
    row_count = lax.axis_size("row")
    col_count = lax.axis_size("col")
    devices = row_count * col_count
    rows_dev, cols_dev = front.shape
    strip_r = child_strips.shape[1]
    strip_c = child_strips.shape[2]
    held = child_strips.shape[0]
    capacity = max(2, 2 * held // devices)
    strips_down = rows_dev // strip_r
    strips_across = cols_dev // strip_c
    local_count = strips_down * strips_across
    owner = child_owner[:, 0]
    positions = jnp.arange(held, dtype=jnp.int32)
    same_owner = owner[:, None] == owner[None, :]
    earlier = positions[:, None] > positions[None, :]
    rank = jnp.sum((same_owner & earlier).astype(jnp.int32), axis=1)
    target = owner * capacity + rank
    route = (target[None, :] == jnp.arange(devices * capacity, dtype=jnp.int32)[:, None]).astype(jnp.float32)
    outgoing = lax.dot_general(
        route,
        child_strips.reshape(held, strip_r * strip_c),
        (((1,), (0,)), ((), ())),
        precision=lax.Precision.HIGHEST,
        preferred_element_type=jnp.float32,
    )
    places = jnp.full((devices * capacity,), local_count, jnp.int32).at[target].set(child_slot)
    arrived, landing = (
        lax.all_to_all(
            outgoing.reshape(devices, capacity, strip_r, strip_c),
            ("row", "col"),
            split_axis=0,
            concat_axis=0,
            tiled=True,
        ),
        lax.all_to_all(
            places.reshape(devices, capacity),
            ("row", "col"),
            split_axis=0,
            concat_axis=0,
            tiled=True,
        ),
    )
    arrived = arrived.reshape(devices * capacity, strip_r, strip_c)
    landing = landing.reshape(devices * capacity)
    row_id = lax.axis_index("row")
    col_id = lax.axis_index("col")
    first_rows = row_id == 0
    is_owner = first_rows & (col_id == 0)

    across = PANEL // strip_c
    srow = landing // strips_across
    scol = landing % strips_across
    hit = (srow < strips_down) & (scol < across)
    spot = jnp.where(hit, srow * across + scol, strips_down * across)
    pick = (spot[None, :] == jnp.arange(strips_down * across, dtype=jnp.int32)[:, None]).astype(jnp.float32)
    part = lax.dot_general(
        pick,
        arrived.reshape(arrived.shape[0], strip_r * strip_c),
        (((1,), (0,)), ((), ())),
        precision=lax.Precision.HIGHEST,
        preferred_element_type=jnp.float32,
    )
    part = part.reshape(strips_down, across, strip_r, strip_c).transpose(0, 2, 1, 3)
    panel_cols = front[:, :PANEL] + part.reshape(rows_dev, PANEL)
    top_block = panel_cols[:PANEL]
    safe_block = jnp.where(
        is_owner, 0.5 * (top_block + top_block.T), jnp.eye(PANEL, dtype=jnp.float32)
    )
    factor11 = jnp.linalg.cholesky(safe_block)

    pieces_l = factor11.reshape(row_count, PANEL // row_count, PANEL)
    held_l = jnp.where(first_rows, pieces_l[0], 0.0)
    for r in range(1, row_count):
        got = lax.ppermute(pieces_l[r], ("row", "col"), [(0, r * col_count)])
        held_l = held_l + got
    factor_col0 = lax.all_gather(held_l, "row", axis=0, tiled=True)

    every = (landing[None, :] == jnp.arange(local_count, dtype=jnp.int32)[:, None]).astype(jnp.float32)
    delta = lax.dot_general(
        every,
        arrived.reshape(arrived.shape[0], strip_r * strip_c),
        (((1,), (0,)), ((), ())),
        precision=lax.Precision.HIGHEST,
        preferred_element_type=jnp.float32,
    )
    delta = delta.reshape(strips_down, strips_across, strip_r, strip_c).transpose(0, 2, 1, 3)
    delta = delta.reshape(rows_dev, cols_dev)

    solved = lax.linalg.triangular_solve(
        factor_col0, panel_cols, left_side=False, lower=True, transpose_a=True
    )
    headed = jnp.concatenate([factor_col0, solved[PANEL:]], axis=0)
    solved = jnp.where(first_rows, headed, solved)
    piece_rows = rows_dev // col_count
    my_piece = solved[:piece_rows]
    for j in range(1, col_count):
        perm = [(k * col_count, k * col_count + j) for k in range(row_count)]
        got = lax.ppermute(solved[j * piece_rows:(j + 1) * piece_rows], ("row", "col"), perm)
        my_piece = jnp.where(col_id == j, got, my_piece)

    ratio = row_count // col_count
    perm = []
    for k in range(row_count):
        c, b = divmod(k, ratio)
        for j in range(col_count):
            perm.append((k * col_count + j, (col_count * b + j) * col_count + c))
    mine = lax.ppermute(my_piece, ("row", "col"), perm)
    column_panel = lax.all_gather(mine, "row", axis=0, tiled=True)
    shifted = [my_piece]
    for s_ in range(1, col_count):
        perm = [
            (k * col_count + j, k * col_count + (j + s_) % col_count)
            for k in range(row_count)
            for j in range(col_count)
        ]
        shifted.append(lax.ppermute(my_piece, ("row", "col"), perm))
    turned = jnp.stack([shifted[(col_count - m) % col_count] for m in range(col_count)] * 2)
    panel_here = lax.dynamic_slice_in_dim(turned, (col_count - col_id) % col_count, col_count, 0)
    panel_here = panel_here.reshape(rows_dev, PANEL)
    update = lax.dot_general(
        panel_here,
        column_panel,
        (((1,), (1,)), ((), ())),
        precision=lax.Precision.HIGH,
        preferred_element_type=jnp.float32,
    )
    global_rows = row_id * rows_dev + jnp.arange(rows_dev, dtype=jnp.int32)
    global_cols = col_id * cols_dev + jnp.arange(cols_dev, dtype=jnp.int32)
    trailing = (global_rows[:, None] >= PANEL) & (global_cols[None, :] >= PANEL)
    factored = (front + delta) - jnp.where(trailing, update, 0.0)
    return (factored, panel_here)


def solution(mesh):
    in_specs = (
        P("row", "col"),
        P(("row", "col"), None, None),
        P(("row", "col"), None),
        P(("row", "col")),
    )
    out_specs = (P("row", "col"), P("row", None))
    return jax.shard_map(shards, mesh=mesh, in_specs=in_specs, out_specs=out_specs, check_vma=False)
```

```python
import jax
import jax.numpy as jnp
from jax import lax
from jax.sharding import PartitionSpec as P

PANEL = 512


def shards(front, child_strips, child_owner, child_slot):
    row_count = lax.axis_size("row")
    col_count = lax.axis_size("col")
    devices = row_count * col_count
    rows_dev, cols_dev = front.shape
    strip_r = child_strips.shape[1]
    strip_c = child_strips.shape[2]
    held = child_strips.shape[0]
    capacity = max(2, 2 * held // devices)
    strips_down = rows_dev // strip_r
    strips_across = cols_dev // strip_c
    local_count = strips_down * strips_across
    owner = child_owner[:, 0]
    positions = jnp.arange(held, dtype=jnp.int32)
    same_owner = owner[:, None] == owner[None, :]
    earlier = positions[:, None] > positions[None, :]
    rank = jnp.sum((same_owner & earlier).astype(jnp.int32), axis=1)
    target = owner * capacity + rank
    flat = strip_r * strip_c
    code = jnp.broadcast_to((child_slot + 1).astype(jnp.float32)[:, None], (held, strip_c))
    payload = jnp.concatenate([child_strips.reshape(held, flat), code], axis=1)
    width = payload.shape[1]
    route = (target[None, :] == jnp.arange(devices * capacity, dtype=jnp.int32)[:, None]).astype(jnp.float32)
    outgoing = lax.dot_general(
        route,
        payload,
        (((1,), (0,)), ((), ())),
        precision=lax.Precision.HIGHEST,
        preferred_element_type=jnp.float32,
    )
    got_all = lax.all_to_all(
        outgoing.reshape(devices, capacity * width),
        ("row", "col"),
        split_axis=0,
        concat_axis=0,
        tiled=True,
    ).reshape(devices * capacity, width)
    arrived = got_all[:, :flat]
    number = jnp.round(got_all[:, flat]).astype(jnp.int32)
    landing = jnp.where(number > 0, number - 1, local_count)
    row_id = lax.axis_index("row")
    col_id = lax.axis_index("col")
    first_rows = row_id == 0
    is_owner = first_rows & (col_id == 0)

    across = PANEL // strip_c
    srow = landing // strips_across
    scol = landing % strips_across
    hit = (srow < strips_down) & (scol < across)
    spot = jnp.where(hit, srow * across + scol, strips_down * across)
    pick = (spot[None, :] == jnp.arange(strips_down * across, dtype=jnp.int32)[:, None]).astype(jnp.float32)
    part = lax.dot_general(
        pick,
        arrived,
        (((1,), (0,)), ((), ())),
        precision=lax.Precision.HIGHEST,
        preferred_element_type=jnp.float32,
    )
    part = part.reshape(strips_down, across, strip_r, strip_c).transpose(0, 2, 1, 3)
    panel_cols = front[:, :PANEL] + part.reshape(rows_dev, PANEL)
    top_block = panel_cols[:PANEL]
    safe_block = jnp.where(
        is_owner, 0.5 * (top_block + top_block.T), jnp.eye(PANEL, dtype=jnp.float32)
    )
    factor11 = jnp.linalg.cholesky(safe_block)

    pieces_l = factor11.reshape(row_count, PANEL // row_count, PANEL)
    held_l = jnp.where(first_rows, pieces_l[0], 0.0)
    for r in range(1, row_count):
        got = lax.ppermute(pieces_l[r], ("row", "col"), [(0, r * col_count)])
        held_l = held_l + got
    factor_col0 = lax.all_gather(held_l, "row", axis=0, tiled=True)

    every = (landing[None, :] == jnp.arange(local_count, dtype=jnp.int32)[:, None]).astype(jnp.float32)
    delta = lax.dot_general(
        every,
        arrived,
        (((1,), (0,)), ((), ())),
        precision=lax.Precision.HIGHEST,
        preferred_element_type=jnp.float32,
    )
    delta = delta.reshape(strips_down, strips_across, strip_r, strip_c).transpose(0, 2, 1, 3)
    delta = delta.reshape(rows_dev, cols_dev)

    solved = lax.linalg.triangular_solve(
        factor_col0, panel_cols, left_side=False, lower=True, transpose_a=True
    )
    headed = jnp.concatenate([factor_col0, solved[PANEL:]], axis=0)
    solved = jnp.where(first_rows, headed, solved)
    piece_rows = rows_dev // col_count
    my_piece = solved[:piece_rows]
    for j in range(1, col_count):
        perm = [(k * col_count, k * col_count + j) for k in range(row_count)]
        got = lax.ppermute(solved[j * piece_rows:(j + 1) * piece_rows], ("row", "col"), perm)
        my_piece = jnp.where(col_id == j, got, my_piece)

    ratio = row_count // col_count
    perm = []
    for k in range(row_count):
        c, b = divmod(k, ratio)
        for j in range(col_count):
            perm.append((k * col_count + j, (col_count * b + j) * col_count + c))
    mine = lax.ppermute(my_piece, ("row", "col"), perm)
    column_panel = lax.all_gather(mine, "row", axis=0, tiled=True)
    shifted = [my_piece]
    for s_ in range(1, col_count):
        perm = [
            (k * col_count + j, k * col_count + (j + s_) % col_count)
            for k in range(row_count)
            for j in range(col_count)
        ]
        shifted.append(lax.ppermute(my_piece, ("row", "col"), perm))
    turned = jnp.stack([shifted[(col_count - m) % col_count] for m in range(col_count)] * 2)
    panel_here = lax.dynamic_slice_in_dim(turned, (col_count - col_id) % col_count, col_count, 0)
    panel_here = panel_here.reshape(rows_dev, PANEL)
    update = lax.dot_general(
        panel_here,
        column_panel,
        (((1,), (1,)), ((), ())),
        precision=lax.Precision.HIGH,
        preferred_element_type=jnp.float32,
    )
    global_rows = row_id * rows_dev + jnp.arange(rows_dev, dtype=jnp.int32)
    global_cols = col_id * cols_dev + jnp.arange(cols_dev, dtype=jnp.int32)
    trailing = (global_rows[:, None] >= PANEL) & (global_cols[None, :] >= PANEL)
    factored = (front + delta) - jnp.where(trailing, update, 0.0)
    return (factored, panel_here)


def solution(mesh):
    in_specs = (
        P("row", "col"),
        P(("row", "col"), None, None),
        P(("row", "col"), None),
        P(("row", "col")),
    )
    out_specs = (P("row", "col"), P("row", None))
    return jax.shard_map(shards, mesh=mesh, in_specs=in_specs, out_specs=out_specs, check_vma=False)
```

```python
import jax
import jax.numpy as jnp
from jax import lax
from jax.sharding import PartitionSpec as P

PANEL = 512


def shards(front, child_strips, child_owner, child_slot):
    row_count = lax.axis_size("row")
    col_count = lax.axis_size("col")
    devices = row_count * col_count
    rows_dev, cols_dev = front.shape
    strip_r = child_strips.shape[1]
    strip_c = child_strips.shape[2]
    held = child_strips.shape[0]
    capacity = max(2, 2 * held // devices)
    strips_down = rows_dev // strip_r
    strips_across = cols_dev // strip_c
    local_count = strips_down * strips_across
    owner = child_owner[:, 0]
    positions = jnp.arange(held, dtype=jnp.int32)
    same_owner = owner[:, None] == owner[None, :]
    earlier = positions[:, None] > positions[None, :]
    rank = jnp.sum((same_owner & earlier).astype(jnp.int32), axis=1)
    target = owner * capacity + rank
    flat = strip_r * strip_c
    code = jnp.broadcast_to((child_slot + 1).astype(jnp.float32)[:, None], (held, strip_c))
    payload = jnp.concatenate([child_strips.reshape(held, flat), code], axis=1)
    width = payload.shape[1]
    route = (target[None, :] == jnp.arange(devices * capacity, dtype=jnp.int32)[:, None]).astype(jnp.float32)
    outgoing = lax.dot_general(
        route,
        payload,
        (((1,), (0,)), ((), ())),
        precision=lax.Precision.HIGHEST,
        preferred_element_type=jnp.float32,
    )
    got_all = lax.all_to_all(
        outgoing.reshape(devices, capacity * width),
        ("row", "col"),
        split_axis=0,
        concat_axis=0,
        tiled=True,
    ).reshape(devices * capacity, width)
    arrived = got_all[:, :flat]
    number = jnp.round(got_all[:, flat]).astype(jnp.int32)
    landing = jnp.where(number > 0, number - 1, local_count)
    row_id = lax.axis_index("row")
    col_id = lax.axis_index("col")
    first_rows = row_id == 0
    is_owner = first_rows & (col_id == 0)

    across = PANEL // strip_c
    srow = landing // strips_across
    scol = landing % strips_across
    hit = (srow < strips_down) & (scol < across)
    spot = jnp.where(hit, srow * across + scol, strips_down * across)
    pick = (spot[None, :] == jnp.arange(strips_down * across, dtype=jnp.int32)[:, None]).astype(jnp.float32)
    part = lax.dot_general(
        pick,
        arrived,
        (((1,), (0,)), ((), ())),
        precision=lax.Precision.HIGHEST,
        preferred_element_type=jnp.float32,
    )
    part = part.reshape(strips_down, across, strip_r, strip_c).transpose(0, 2, 1, 3)
    panel_cols = front[:, :PANEL] + part.reshape(rows_dev, PANEL)
    top_block = panel_cols[:PANEL]
    safe_block = jnp.where(
        is_owner, 0.5 * (top_block + top_block.T), jnp.eye(PANEL, dtype=jnp.float32)
    )
    factor11 = jnp.linalg.cholesky(safe_block)

    group = 4 if row_count % 4 == 0 else 1
    factor_col0 = factor11
    for m in range(1, row_count // group):
        got = lax.ppermute(factor11, ("row", "col"), [(0, m * group * col_count)])
        factor_col0 = jnp.where(row_id == m * group, got, factor_col0)
    lead = factor_col0
    for z in range(1, group):
        perm = [(m * group * col_count, (m * group + z) * col_count) for m in range(row_count // group)]
        got = lax.ppermute(lead, ("row", "col"), perm)
        factor_col0 = jnp.where(row_id % group == z, got, factor_col0)

    every = (landing[None, :] == jnp.arange(local_count, dtype=jnp.int32)[:, None]).astype(jnp.float32)
    delta = lax.dot_general(
        every,
        arrived,
        (((1,), (0,)), ((), ())),
        precision=lax.Precision.HIGHEST,
        preferred_element_type=jnp.float32,
    )
    delta = delta.reshape(strips_down, strips_across, strip_r, strip_c).transpose(0, 2, 1, 3)
    delta = delta.reshape(rows_dev, cols_dev)

    solved = lax.linalg.triangular_solve(
        factor_col0, panel_cols, left_side=False, lower=True, transpose_a=True
    )
    headed = jnp.concatenate([factor_col0, solved[PANEL:]], axis=0)
    solved = jnp.where(first_rows, headed, solved)
    piece_rows = rows_dev // col_count
    my_piece = solved[:piece_rows]
    for j in range(1, col_count):
        perm = [(k * col_count, k * col_count + j) for k in range(row_count)]
        got = lax.ppermute(solved[j * piece_rows:(j + 1) * piece_rows], ("row", "col"), perm)
        my_piece = jnp.where(col_id == j, got, my_piece)

    ratio = row_count // col_count
    perm = []
    for k in range(row_count):
        c, b = divmod(k, ratio)
        for j in range(col_count):
            perm.append((k * col_count + j, (col_count * b + j) * col_count + c))
    mine = lax.ppermute(my_piece, ("row", "col"), perm)
    column_panel = lax.all_gather(mine, "row", axis=0, tiled=True)
    shifted = [my_piece]
    for s_ in range(1, col_count):
        perm = [
            (k * col_count + j, k * col_count + (j + s_) % col_count)
            for k in range(row_count)
            for j in range(col_count)
        ]
        shifted.append(lax.ppermute(my_piece, ("row", "col"), perm))
    turned = jnp.stack([shifted[(col_count - m) % col_count] for m in range(col_count)] * 2)
    panel_here = lax.dynamic_slice_in_dim(turned, (col_count - col_id) % col_count, col_count, 0)
    panel_here = panel_here.reshape(rows_dev, PANEL)
    update = lax.dot_general(
        panel_here,
        column_panel,
        (((1,), (1,)), ((), ())),
        precision=lax.Precision.HIGH,
        preferred_element_type=jnp.float32,
    )
    global_rows = row_id * rows_dev + jnp.arange(rows_dev, dtype=jnp.int32)
    global_cols = col_id * cols_dev + jnp.arange(cols_dev, dtype=jnp.int32)
    trailing = (global_rows[:, None] >= PANEL) & (global_cols[None, :] >= PANEL)
    factored = (front + delta) - jnp.where(trailing, update, 0.0)
    return (factored, panel_here)


def solution(mesh):
    in_specs = (
        P("row", "col"),
        P(("row", "col"), None, None),
        P(("row", "col"), None),
        P(("row", "col")),
    )
    out_specs = (P("row", "col"), P("row", None))
    return jax.shard_map(shards, mesh=mesh, in_specs=in_specs, out_specs=out_specs, check_vma=False)
```

```python
import jax
import jax.numpy as jnp
from jax import lax
from jax.sharding import PartitionSpec as P

PANEL = 512


def shards(front, child_strips, child_owner, child_slot):
    row_count = lax.axis_size("row")
    col_count = lax.axis_size("col")
    devices = row_count * col_count
    rows_dev, cols_dev = front.shape
    strip_r = child_strips.shape[1]
    strip_c = child_strips.shape[2]
    held = child_strips.shape[0]
    capacity = max(2, 2 * held // devices)
    strips_down = rows_dev // strip_r
    strips_across = cols_dev // strip_c
    local_count = strips_down * strips_across
    owner = child_owner[:, 0]
    positions = jnp.arange(held, dtype=jnp.int32)
    same_owner = owner[:, None] == owner[None, :]
    earlier = positions[:, None] > positions[None, :]
    rank = jnp.sum((same_owner & earlier).astype(jnp.int32), axis=1)
    target = owner * capacity + rank
    flat = strip_r * strip_c
    code = jnp.broadcast_to((child_slot + 1).astype(jnp.float32)[:, None], (held, strip_c))
    payload = jnp.concatenate([child_strips.reshape(held, flat), code], axis=1)
    width = payload.shape[1]
    route = (target[None, :] == jnp.arange(devices * capacity, dtype=jnp.int32)[:, None]).astype(jnp.float32)
    outgoing = lax.dot_general(
        route,
        payload,
        (((1,), (0,)), ((), ())),
        precision=lax.Precision.HIGHEST,
        preferred_element_type=jnp.float32,
    )
    got_all = lax.all_to_all(
        outgoing.reshape(devices, capacity * width),
        ("row", "col"),
        split_axis=0,
        concat_axis=0,
        tiled=True,
    ).reshape(devices * capacity, width)
    arrived = got_all[:, :flat]
    number = jnp.round(got_all[:, flat]).astype(jnp.int32)
    landing = jnp.where(number > 0, number - 1, local_count)
    row_id = lax.axis_index("row")
    col_id = lax.axis_index("col")
    first_rows = row_id == 0
    is_owner = first_rows & (col_id == 0)

    across = PANEL // strip_c
    srow = landing // strips_across
    scol = landing % strips_across
    hit = (srow < strips_down) & (scol < across)
    spot = jnp.where(hit, srow * across + scol, strips_down * across)
    pick = (spot[None, :] == jnp.arange(strips_down * across, dtype=jnp.int32)[:, None]).astype(jnp.float32)
    part = lax.dot_general(
        pick,
        arrived,
        (((1,), (0,)), ((), ())),
        precision=lax.Precision.HIGHEST,
        preferred_element_type=jnp.float32,
    )
    part = part.reshape(strips_down, across, strip_r, strip_c).transpose(0, 2, 1, 3)
    panel_cols = front[:, :PANEL] + part.reshape(rows_dev, PANEL)
    top_block = panel_cols[:PANEL]
    safe_block = jnp.where(
        is_owner, 0.5 * (top_block + top_block.T), jnp.eye(PANEL, dtype=jnp.float32)
    )
    factor11 = jnp.linalg.cholesky(safe_block)

    group = 4 if row_count % 4 == 0 else 1
    factor_col0 = factor11
    for m in range(1, row_count // group):
        got = lax.ppermute(factor11, ("row", "col"), [(0, m * group * col_count)])
        factor_col0 = jnp.where(row_id == m * group, got, factor_col0)
    lead = factor_col0
    for z in range(1, group):
        perm = [(m * group * col_count, (m * group + z) * col_count) for m in range(row_count // group)]
        got = lax.ppermute(lead, ("row", "col"), perm)
        factor_col0 = jnp.where(row_id % group == z, got, factor_col0)

    every = (landing[None, :] == jnp.arange(local_count, dtype=jnp.int32)[:, None]).astype(jnp.float32)
    delta = lax.dot_general(
        every,
        arrived,
        (((1,), (0,)), ((), ())),
        precision=lax.Precision.HIGHEST,
        preferred_element_type=jnp.float32,
    )
    delta = delta.reshape(strips_down, strips_across, strip_r, strip_c).transpose(0, 2, 1, 3)
    delta = delta.reshape(rows_dev, cols_dev)

    solved = lax.linalg.triangular_solve(
        factor_col0, panel_cols, left_side=False, lower=True, transpose_a=True
    )
    headed = jnp.concatenate([factor_col0, solved[PANEL:]], axis=0)
    solved = jnp.where(first_rows, headed, solved)
    piece_rows = rows_dev // col_count
    my_piece = solved[:piece_rows]
    for j in range(1, col_count):
        perm = [(k * col_count, k * col_count + j) for k in range(row_count)]
        got = lax.ppermute(solved[j * piece_rows:(j + 1) * piece_rows], ("row", "col"), perm)
        my_piece = jnp.where(col_id == j, got, my_piece)

    ratio = row_count // col_count
    perm = []
    for k in range(row_count):
        c, b = divmod(k, ratio)
        for j in range(col_count):
            perm.append((k * col_count + j, (col_count * b + j) * col_count + c))
    mine = lax.ppermute(my_piece, ("row", "col"), perm)
    moved = [mine]
    for s_ in range(1, row_count):
        perm = [
            (k * col_count + j, ((k + s_) % row_count) * col_count + j)
            for k in range(row_count)
            for j in range(col_count)
        ]
        moved.append(lax.ppermute(mine, ("row", "col"), perm))
    turned_rows = jnp.stack([moved[(row_count - m) % row_count] for m in range(row_count)] * 2)
    column_panel = lax.dynamic_slice_in_dim(turned_rows, (row_count - row_id) % row_count, row_count, 0)
    column_panel = column_panel.reshape(row_count * piece_rows, PANEL)
    shifted = [my_piece]
    for s_ in range(1, col_count):
        perm = [
            (k * col_count + j, k * col_count + (j + s_) % col_count)
            for k in range(row_count)
            for j in range(col_count)
        ]
        shifted.append(lax.ppermute(my_piece, ("row", "col"), perm))
    turned = jnp.stack([shifted[(col_count - m) % col_count] for m in range(col_count)] * 2)
    panel_here = lax.dynamic_slice_in_dim(turned, (col_count - col_id) % col_count, col_count, 0)
    panel_here = panel_here.reshape(rows_dev, PANEL)
    update = lax.dot_general(
        panel_here,
        column_panel,
        (((1,), (1,)), ((), ())),
        precision=lax.Precision.HIGH,
        preferred_element_type=jnp.float32,
    )
    global_rows = row_id * rows_dev + jnp.arange(rows_dev, dtype=jnp.int32)
    global_cols = col_id * cols_dev + jnp.arange(cols_dev, dtype=jnp.int32)
    trailing = (global_rows[:, None] >= PANEL) & (global_cols[None, :] >= PANEL)
    factored = (front + delta) - jnp.where(trailing, update, 0.0)
    return (factored, panel_here)


def solution(mesh):
    in_specs = (
        P("row", "col"),
        P(("row", "col"), None, None),
        P(("row", "col"), None),
        P(("row", "col")),
    )
    out_specs = (P("row", "col"), P("row", None))
    return jax.shard_map(shards, mesh=mesh, in_specs=in_specs, out_specs=out_specs, check_vma=False)
```

```python
import jax
import jax.numpy as jnp
from jax import lax
from jax.sharding import PartitionSpec as P

PANEL = 512


def shards(front, child_strips, child_owner, child_slot):
    row_count = lax.axis_size("row")
    col_count = lax.axis_size("col")
    devices = row_count * col_count
    rows_dev, cols_dev = front.shape
    strip_r = child_strips.shape[1]
    strip_c = child_strips.shape[2]
    held = child_strips.shape[0]
    capacity = max(2, 2 * held // devices)
    strips_down = rows_dev // strip_r
    strips_across = cols_dev // strip_c
    local_count = strips_down * strips_across
    owner = child_owner[:, 0]
    positions = jnp.arange(held, dtype=jnp.int32)
    same_owner = owner[:, None] == owner[None, :]
    earlier = positions[:, None] > positions[None, :]
    rank = jnp.sum((same_owner & earlier).astype(jnp.int32), axis=1)
    target = owner * capacity + rank
    flat = strip_r * strip_c
    code = jnp.broadcast_to((child_slot + 1).astype(jnp.float32)[:, None], (held, strip_c))
    payload = jnp.concatenate([child_strips.reshape(held, flat), code], axis=1)
    width = payload.shape[1]
    route = (target[None, :] == jnp.arange(devices * capacity, dtype=jnp.int32)[:, None]).astype(jnp.float32)
    outgoing = lax.dot_general(
        route,
        payload,
        (((1,), (0,)), ((), ())),
        precision=lax.Precision.HIGHEST,
        preferred_element_type=jnp.float32,
    )
    got_all = lax.all_to_all(
        outgoing.reshape(devices, capacity * width),
        ("row", "col"),
        split_axis=0,
        concat_axis=0,
        tiled=True,
    ).reshape(devices * capacity, width)
    arrived = got_all[:, :flat]
    number = jnp.round(got_all[:, flat]).astype(jnp.int32)
    landing = jnp.where(number > 0, number - 1, local_count)
    row_id = lax.axis_index("row")
    col_id = lax.axis_index("col")
    first_rows = row_id == 0
    is_owner = first_rows & (col_id == 0)

    across = PANEL // strip_c
    srow = landing // strips_across
    scol = landing % strips_across
    hit = (srow < strips_down) & (scol < across)
    spot = jnp.where(hit, srow * across + scol, strips_down * across)
    pick = (spot[None, :] == jnp.arange(strips_down * across, dtype=jnp.int32)[:, None]).astype(jnp.float32)
    part = lax.dot_general(
        pick,
        arrived,
        (((1,), (0,)), ((), ())),
        precision=lax.Precision.HIGHEST,
        preferred_element_type=jnp.float32,
    )
    part = part.reshape(strips_down, across, strip_r, strip_c).transpose(0, 2, 1, 3)
    panel_cols = front[:, :PANEL] + part.reshape(rows_dev, PANEL)
    top_block = panel_cols[:PANEL]
    safe_block = jnp.where(
        is_owner, 0.5 * (top_block + top_block.T), jnp.eye(PANEL, dtype=jnp.float32)
    )
    factor11 = jnp.linalg.cholesky(safe_block)

    band = PANEL // 4
    sent = tuple(factor11[i * band:(i + 1) * band, :(i + 1) * band] for i in range(4))
    group = 4 if row_count % 4 == 0 else 1
    held_l = sent
    for m in range(1, row_count // group):
        got = lax.ppermute(sent, ("row", "col"), [(0, m * group * col_count)])
        held_l = tuple(jnp.where(row_id == m * group, g, h) for g, h in zip(got, held_l))
    lead = held_l
    for z in range(1, group):
        perm = [(m * group * col_count, (m * group + z) * col_count) for m in range(row_count // group)]
        got = lax.ppermute(lead, ("row", "col"), perm)
        held_l = tuple(jnp.where(row_id % group == z, g, h) for g, h in zip(got, held_l))
    factor_col0 = jnp.concatenate(
        [jnp.pad(p, ((0, 0), (0, PANEL - p.shape[1]))) for p in held_l], axis=0
    )

    every = (landing[None, :] == jnp.arange(local_count, dtype=jnp.int32)[:, None]).astype(jnp.float32)
    delta = lax.dot_general(
        every,
        arrived,
        (((1,), (0,)), ((), ())),
        precision=lax.Precision.HIGHEST,
        preferred_element_type=jnp.float32,
    )
    delta = delta.reshape(strips_down, strips_across, strip_r, strip_c).transpose(0, 2, 1, 3)
    delta = delta.reshape(rows_dev, cols_dev)

    solved = lax.linalg.triangular_solve(
        factor_col0, panel_cols, left_side=False, lower=True, transpose_a=True
    )
    headed = jnp.concatenate([factor11, solved[PANEL:]], axis=0)
    solved = jnp.where(first_rows, headed, solved)
    piece_rows = rows_dev // col_count
    my_piece = solved[:piece_rows]
    for j in range(1, col_count):
        perm = [(k * col_count, k * col_count + j) for k in range(row_count)]
        got = lax.ppermute(solved[j * piece_rows:(j + 1) * piece_rows], ("row", "col"), perm)
        my_piece = jnp.where(col_id == j, got, my_piece)

    ratio = row_count // col_count
    perm = []
    for k in range(row_count):
        c, b = divmod(k, ratio)
        for j in range(col_count):
            perm.append((k * col_count + j, (col_count * b + j) * col_count + c))
    mine = lax.ppermute(my_piece, ("row", "col"), perm)
    column_panel = lax.all_gather(mine, "row", axis=0, tiled=True)
    shifted = [my_piece]
    for s_ in range(1, col_count):
        perm = [
            (k * col_count + j, k * col_count + (j + s_) % col_count)
            for k in range(row_count)
            for j in range(col_count)
        ]
        shifted.append(lax.ppermute(my_piece, ("row", "col"), perm))
    turned = jnp.stack([shifted[(col_count - m) % col_count] for m in range(col_count)] * 2)
    panel_here = lax.dynamic_slice_in_dim(turned, (col_count - col_id) % col_count, col_count, 0)
    panel_here = panel_here.reshape(rows_dev, PANEL)
    update = lax.dot_general(
        panel_here,
        column_panel,
        (((1,), (1,)), ((), ())),
        precision=lax.Precision.HIGH,
        preferred_element_type=jnp.float32,
    )
    global_rows = row_id * rows_dev + jnp.arange(rows_dev, dtype=jnp.int32)
    global_cols = col_id * cols_dev + jnp.arange(cols_dev, dtype=jnp.int32)
    trailing = (global_rows[:, None] >= PANEL) & (global_cols[None, :] >= PANEL)
    factored = (front + delta) - jnp.where(trailing, update, 0.0)
    return (factored, panel_here)


def solution(mesh):
    in_specs = (
        P("row", "col"),
        P(("row", "col"), None, None),
        P(("row", "col"), None),
        P(("row", "col")),
    )
    out_specs = (P("row", "col"), P("row", None))
    return jax.shard_map(shards, mesh=mesh, in_specs=in_specs, out_specs=out_specs, check_vma=False)
```

```python
import jax
import jax.numpy as jnp
from jax import lax
from jax.sharding import PartitionSpec as P

PANEL = 512


def shards(front, child_strips, child_owner, child_slot):
    row_count = lax.axis_size("row")
    col_count = lax.axis_size("col")
    devices = row_count * col_count
    rows_dev, cols_dev = front.shape
    strip_r = child_strips.shape[1]
    strip_c = child_strips.shape[2]
    held = child_strips.shape[0]
    capacity = max(2, 2 * held // devices)
    strips_down = rows_dev // strip_r
    strips_across = cols_dev // strip_c
    local_count = strips_down * strips_across
    owner = child_owner[:, 0]
    positions = jnp.arange(held, dtype=jnp.int32)
    same_owner = owner[:, None] == owner[None, :]
    earlier = positions[:, None] > positions[None, :]
    rank = jnp.sum((same_owner & earlier).astype(jnp.int32), axis=1)
    target = owner * capacity + rank
    flat = strip_r * strip_c
    code = jnp.broadcast_to((child_slot + 1).astype(jnp.float32)[:, None], (held, strip_c))
    payload = jnp.concatenate([child_strips.reshape(held, flat), code], axis=1)
    width = payload.shape[1]
    route = (target[None, :] == jnp.arange(devices * capacity, dtype=jnp.int32)[:, None]).astype(jnp.float32)
    outgoing = lax.dot_general(
        route,
        payload,
        (((1,), (0,)), ((), ())),
        precision=lax.Precision.HIGHEST,
        preferred_element_type=jnp.float32,
    )
    got_all = lax.all_to_all(
        outgoing.reshape(devices, capacity * width),
        ("row", "col"),
        split_axis=0,
        concat_axis=0,
        tiled=True,
    ).reshape(devices * capacity, width)
    arrived = got_all[:, :flat]
    number = jnp.round(got_all[:, flat]).astype(jnp.int32)
    landing = jnp.where(number > 0, number - 1, local_count)
    row_id = lax.axis_index("row")
    col_id = lax.axis_index("col")
    first_rows = row_id == 0
    is_owner = first_rows & (col_id == 0)

    across = PANEL // strip_c
    srow = landing // strips_across
    scol = landing % strips_across
    hit = (srow < strips_down) & (scol < across)
    spot = jnp.where(hit, srow * across + scol, strips_down * across)
    pick = (spot[None, :] == jnp.arange(strips_down * across, dtype=jnp.int32)[:, None]).astype(jnp.float32)
    part = lax.dot_general(
        pick,
        arrived,
        (((1,), (0,)), ((), ())),
        precision=lax.Precision.HIGHEST,
        preferred_element_type=jnp.float32,
    )
    part = part.reshape(strips_down, across, strip_r, strip_c).transpose(0, 2, 1, 3)
    panel_cols = front[:, :PANEL] + part.reshape(rows_dev, PANEL)
    top_block = panel_cols[:PANEL]
    safe_block = jnp.where(
        is_owner, 0.5 * (top_block + top_block.T), jnp.eye(PANEL, dtype=jnp.float32)
    )
    factor11 = jnp.linalg.cholesky(safe_block)

    bands = 8
    band = PANEL // bands
    sent = tuple(factor11[i * band:(i + 1) * band, :(i + 1) * band] for i in range(bands))
    group = 4 if row_count % 4 == 0 else 1
    relay = 1 if col_count > 1 and group > 1 else 0
    held_l = sent
    if relay:
        got = lax.ppermute(sent, ("row", "col"), [(0, relay)])
        held_l = tuple(jnp.where(col_id == relay, g, h) for g, h in zip(got, held_l))
    for m in range(1, row_count // group):
        got = lax.ppermute(sent, ("row", "col"), [(0, m * group * col_count)])
        held_l = tuple(jnp.where(row_id == m * group, g, h) for g, h in zip(got, held_l))
    lead = held_l
    for z in range(1, group):
        perm = [
            (relay if m == 0 else m * group * col_count, (m * group + z) * col_count)
            for m in range(row_count // group)
        ]
        got = lax.ppermute(lead, ("row", "col"), perm)
        held_l = tuple(jnp.where((row_id % group == z) & (col_id == 0), g, h) for g, h in zip(got, held_l))
    factor_col0 = jnp.concatenate(
        [jnp.pad(p, ((0, 0), (0, PANEL - p.shape[1]))) for p in held_l], axis=0
    )

    every = (landing[None, :] == jnp.arange(local_count, dtype=jnp.int32)[:, None]).astype(jnp.float32)
    delta = lax.dot_general(
        every,
        arrived,
        (((1,), (0,)), ((), ())),
        precision=lax.Precision.HIGHEST,
        preferred_element_type=jnp.float32,
    )
    delta = delta.reshape(strips_down, strips_across, strip_r, strip_c).transpose(0, 2, 1, 3)
    delta = delta.reshape(rows_dev, cols_dev)

    solved = lax.linalg.triangular_solve(
        factor_col0, panel_cols, left_side=False, lower=True, transpose_a=True
    )
    headed = jnp.concatenate([factor11, solved[PANEL:]], axis=0)
    solved = jnp.where(first_rows, headed, solved)
    piece_rows = rows_dev // col_count
    my_piece = solved[:piece_rows]
    for j in range(1, col_count):
        perm = [(k * col_count, k * col_count + j) for k in range(row_count)]
        got = lax.ppermute(solved[j * piece_rows:(j + 1) * piece_rows], ("row", "col"), perm)
        my_piece = jnp.where(col_id == j, got, my_piece)

    ratio = row_count // col_count
    perm = []
    for k in range(row_count):
        c, b = divmod(k, ratio)
        for j in range(col_count):
            perm.append((k * col_count + j, (col_count * b + j) * col_count + c))
    mine = lax.ppermute(my_piece, ("row", "col"), perm)
    column_panel = lax.all_gather(mine, "row", axis=0, tiled=True)
    shifted = [my_piece]
    for s_ in range(1, col_count):
        perm = [
            (k * col_count + j, k * col_count + (j + s_) % col_count)
            for k in range(row_count)
            for j in range(col_count)
        ]
        shifted.append(lax.ppermute(my_piece, ("row", "col"), perm))
    turned = jnp.stack([shifted[(col_count - m) % col_count] for m in range(col_count)] * 2)
    panel_here = lax.dynamic_slice_in_dim(turned, (col_count - col_id) % col_count, col_count, 0)
    panel_here = panel_here.reshape(rows_dev, PANEL)
    update = lax.dot_general(
        panel_here,
        column_panel,
        (((1,), (1,)), ((), ())),
        precision=lax.Precision.HIGH,
        preferred_element_type=jnp.float32,
    )
    global_rows = row_id * rows_dev + jnp.arange(rows_dev, dtype=jnp.int32)
    global_cols = col_id * cols_dev + jnp.arange(cols_dev, dtype=jnp.int32)
    trailing = (global_rows[:, None] >= PANEL) & (global_cols[None, :] >= PANEL)
    factored = (front + delta) - jnp.where(trailing, update, 0.0)
    return (factored, panel_here)


def solution(mesh):
    in_specs = (
        P("row", "col"),
        P(("row", "col"), None, None),
        P(("row", "col"), None),
        P(("row", "col")),
    )
    out_specs = (P("row", "col"), P("row", None))
    return jax.shard_map(shards, mesh=mesh, in_specs=in_specs, out_specs=out_specs, check_vma=False)
```

```python
import jax
import jax.numpy as jnp
from jax import lax
from jax.sharding import PartitionSpec as P

PANEL = 512


def shards(front, child_strips, child_owner, child_slot):
    row_count = lax.axis_size("row")
    col_count = lax.axis_size("col")
    devices = row_count * col_count
    rows_dev, cols_dev = front.shape
    strip_r = child_strips.shape[1]
    strip_c = child_strips.shape[2]
    held = child_strips.shape[0]
    capacity = max(2, 2 * held // devices)
    strips_down = rows_dev // strip_r
    strips_across = cols_dev // strip_c
    local_count = strips_down * strips_across
    owner = child_owner[:, 0]
    positions = jnp.arange(held, dtype=jnp.int32)
    same_owner = owner[:, None] == owner[None, :]
    earlier = positions[:, None] > positions[None, :]
    rank = jnp.sum((same_owner & earlier).astype(jnp.int32), axis=1)
    target = owner * capacity + rank
    flat = strip_r * strip_c
    code = jnp.broadcast_to((child_slot + 1).astype(jnp.float32)[:, None], (held, strip_c))
    payload = jnp.concatenate([child_strips.reshape(held, flat), code], axis=1)
    width = payload.shape[1]
    route = (target[None, :] == jnp.arange(devices * capacity, dtype=jnp.int32)[:, None]).astype(jnp.float32)
    outgoing = lax.dot_general(
        route,
        payload,
        (((1,), (0,)), ((), ())),
        precision=lax.Precision.HIGHEST,
        preferred_element_type=jnp.float32,
    )
    got_all = lax.all_to_all(
        outgoing.reshape(devices, capacity * width),
        ("row", "col"),
        split_axis=0,
        concat_axis=0,
        tiled=True,
    ).reshape(devices * capacity, width)
    arrived = got_all[:, :flat]
    number = jnp.round(got_all[:, flat]).astype(jnp.int32)
    landing = jnp.where(number > 0, number - 1, local_count)
    row_id = lax.axis_index("row")
    col_id = lax.axis_index("col")
    first_rows = row_id == 0
    is_owner = first_rows & (col_id == 0)

    across = PANEL // strip_c
    srow = landing // strips_across
    scol = landing % strips_across
    hit = (srow < strips_down) & (scol < across)
    spot = jnp.where(hit, srow * across + scol, strips_down * across)
    pick = (spot[None, :] == jnp.arange(strips_down * across, dtype=jnp.int32)[:, None]).astype(jnp.float32)
    part = lax.dot_general(
        pick,
        arrived,
        (((1,), (0,)), ((), ())),
        precision=lax.Precision.HIGHEST,
        preferred_element_type=jnp.float32,
    )
    part = part.reshape(strips_down, across, strip_r, strip_c).transpose(0, 2, 1, 3)
    panel_cols = front[:, :PANEL] + part.reshape(rows_dev, PANEL)
    top_block = panel_cols[:PANEL]
    safe_block = jnp.where(
        is_owner, 0.5 * (top_block + top_block.T), jnp.eye(PANEL, dtype=jnp.float32)
    )
    factor11 = jnp.linalg.cholesky(safe_block)

    bands = 8
    band = PANEL // bands
    sent = tuple(factor11[i * band:(i + 1) * band, :(i + 1) * band] for i in range(bands))
    group = 4 if row_count % 4 == 0 else 1
    held_l = sent
    for m in range(1, row_count // group):
        got = lax.ppermute(sent, ("row", "col"), [(0, m * group * col_count)])
        held_l = tuple(jnp.where(row_id == m * group, g, h) for g, h in zip(got, held_l))
    lead = held_l
    for z in range(1, group):
        perm = [(m * group * col_count, (m * group + z) * col_count) for m in range(row_count // group)]
        got = lax.ppermute(lead, ("row", "col"), perm)
        held_l = tuple(jnp.where(row_id % group == z, g, h) for g, h in zip(got, held_l))
    factor_col0 = jnp.concatenate(
        [jnp.pad(p, ((0, 0), (0, PANEL - p.shape[1]))) for p in held_l], axis=0
    )

    every = (landing[None, :] == jnp.arange(local_count, dtype=jnp.int32)[:, None]).astype(jnp.float32)
    delta = lax.dot_general(
        every,
        arrived,
        (((1,), (0,)), ((), ())),
        precision=lax.Precision.HIGHEST,
        preferred_element_type=jnp.float32,
    )
    delta = delta.reshape(strips_down, strips_across, strip_r, strip_c).transpose(0, 2, 1, 3)
    delta = delta.reshape(rows_dev, cols_dev)

    solved = lax.linalg.triangular_solve(
        factor_col0, panel_cols, left_side=False, lower=True, transpose_a=True
    )
    headed = jnp.concatenate([factor11, solved[PANEL:]], axis=0)
    solved = jnp.where(first_rows, headed, solved)
    piece_rows = rows_dev // col_count
    my_piece = solved[:piece_rows]
    for j in range(1, col_count):
        perm = [(k * col_count, k * col_count + j) for k in range(row_count)]
        got = lax.ppermute(solved[j * piece_rows:(j + 1) * piece_rows], ("row", "col"), perm)
        my_piece = jnp.where(col_id == j, got, my_piece)

    ratio = row_count // col_count
    perm = []
    for k in range(row_count):
        c, b = divmod(k, ratio)
        for j in range(col_count):
            perm.append((k * col_count + j, (col_count * b + j) * col_count + c))
    mine = lax.ppermute(my_piece, ("row", "col"), perm)
    column_panel = lax.all_gather(mine, "row", axis=0, tiled=True)
    shifted = [my_piece]
    for s_ in range(1, col_count):
        perm = [
            (k * col_count + j, k * col_count + (j + s_) % col_count)
            for k in range(row_count)
            for j in range(col_count)
        ]
        shifted.append(lax.ppermute(my_piece, ("row", "col"), perm))
    turned = jnp.stack([shifted[(col_count - m) % col_count] for m in range(col_count)] * 2)
    panel_here = lax.dynamic_slice_in_dim(turned, (col_count - col_id) % col_count, col_count, 0)
    panel_here = panel_here.reshape(rows_dev, PANEL)
    update = lax.dot_general(
        panel_here,
        column_panel,
        (((1,), (1,)), ((), ())),
        precision=lax.Precision.HIGH,
        preferred_element_type=jnp.float32,
    )
    global_rows = row_id * rows_dev + jnp.arange(rows_dev, dtype=jnp.int32)
    global_cols = col_id * cols_dev + jnp.arange(cols_dev, dtype=jnp.int32)
    trailing = (global_rows[:, None] >= PANEL) & (global_cols[None, :] >= PANEL)
    factored = (front + delta) - jnp.where(trailing, update, 0.0)
    return (factored, panel_here)


def solution(mesh):
    in_specs = (
        P("row", "col"),
        P(("row", "col"), None, None),
        P(("row", "col"), None),
        P(("row", "col")),
    )
    out_specs = (P("row", "col"), P("row", None))
    return jax.shard_map(shards, mesh=mesh, in_specs=in_specs, out_specs=out_specs, check_vma=False)
```

```python
import jax
import jax.numpy as jnp
from jax import lax
from jax.sharding import PartitionSpec as P

PANEL = 512


def shards(front, child_strips, child_owner, child_slot):
    row_count = lax.axis_size("row")
    col_count = lax.axis_size("col")
    devices = row_count * col_count
    rows_dev, cols_dev = front.shape
    strip_r = child_strips.shape[1]
    strip_c = child_strips.shape[2]
    held = child_strips.shape[0]
    capacity = max(2, 2 * held // devices)
    strips_down = rows_dev // strip_r
    strips_across = cols_dev // strip_c
    local_count = strips_down * strips_across
    owner = child_owner[:, 0]
    positions = jnp.arange(held, dtype=jnp.int32)
    same_owner = owner[:, None] == owner[None, :]
    earlier = positions[:, None] > positions[None, :]
    rank = jnp.sum((same_owner & earlier).astype(jnp.int32), axis=1)
    target = owner * capacity + rank
    flat = strip_r * strip_c
    code = jnp.broadcast_to((child_slot + 1).astype(jnp.float32)[:, None], (held, strip_c))
    payload = jnp.concatenate([child_strips.reshape(held, flat), code], axis=1)
    width = payload.shape[1]
    route = (target[None, :] == jnp.arange(devices * capacity, dtype=jnp.int32)[:, None]).astype(jnp.float32)
    outgoing = lax.dot_general(
        route,
        payload,
        (((1,), (0,)), ((), ())),
        precision=lax.Precision.HIGHEST,
        preferred_element_type=jnp.float32,
    )
    got_all = lax.all_to_all(
        outgoing.reshape(devices, capacity * width),
        ("row", "col"),
        split_axis=0,
        concat_axis=0,
        tiled=True,
    ).reshape(devices * capacity, width)
    arrived = got_all[:, :flat]
    number = jnp.round(got_all[:, flat]).astype(jnp.int32)
    landing = jnp.where(number > 0, number - 1, local_count)
    row_id = lax.axis_index("row")
    col_id = lax.axis_index("col")
    first_rows = row_id == 0
    is_owner = first_rows & (col_id == 0)

    across = PANEL // strip_c
    srow = landing // strips_across
    scol = landing % strips_across
    hit = (srow < strips_down) & (scol < across)
    spot = jnp.where(hit, srow * across + scol, strips_down * across)
    pick = (spot[None, :] == jnp.arange(strips_down * across, dtype=jnp.int32)[:, None]).astype(jnp.float32)
    part = lax.dot_general(
        pick,
        arrived,
        (((1,), (0,)), ((), ())),
        precision=lax.Precision.HIGHEST,
        preferred_element_type=jnp.float32,
    )
    part = part.reshape(strips_down, across, strip_r, strip_c).transpose(0, 2, 1, 3)
    panel_cols = front[:, :PANEL] + part.reshape(rows_dev, PANEL)
    top_block = panel_cols[:PANEL]
    safe_block = jnp.where(
        is_owner, 0.5 * (top_block + top_block.T), jnp.eye(PANEL, dtype=jnp.float32)
    )
    factor11 = jnp.linalg.cholesky(safe_block)

    band = PANEL // 4
    low = [factor11[i * band:(i + 1) * band, :(i + 1) * band] for i in range(4)]
    sent = jnp.concatenate(
        [jnp.concatenate([low[0], low[2]], axis=1), low[3], low[1].reshape(band // 2, PANEL)], axis=0
    )
    group = 4 if row_count % 4 == 0 else 1
    held_l = sent
    for m in range(1, row_count // group):
        got = lax.ppermute(sent, ("row", "col"), [(0, m * group * col_count)])
        held_l = jnp.where(row_id == m * group, got, held_l)
    lead = held_l
    for z in range(1, group):
        perm = [(m * group * col_count, (m * group + z) * col_count) for m in range(row_count // group)]
        got = lax.ppermute(lead, ("row", "col"), perm)
        held_l = jnp.where(row_id % group == z, got, held_l)
    parts = [
        held_l[:band, :band],
        held_l[2 * band:2 * band + band // 2].reshape(band, 2 * band),
        held_l[:band, band:],
        held_l[band:2 * band],
    ]
    factor_col0 = jnp.concatenate(
        [jnp.pad(p, ((0, 0), (0, PANEL - p.shape[1]))) for p in parts], axis=0
    )

    every = (landing[None, :] == jnp.arange(local_count, dtype=jnp.int32)[:, None]).astype(jnp.float32)
    delta = lax.dot_general(
        every,
        arrived,
        (((1,), (0,)), ((), ())),
        precision=lax.Precision.HIGHEST,
        preferred_element_type=jnp.float32,
    )
    delta = delta.reshape(strips_down, strips_across, strip_r, strip_c).transpose(0, 2, 1, 3)
    delta = delta.reshape(rows_dev, cols_dev)

    solved = lax.linalg.triangular_solve(
        factor_col0, panel_cols, left_side=False, lower=True, transpose_a=True
    )
    headed = jnp.concatenate([factor11, solved[PANEL:]], axis=0)
    solved = jnp.where(first_rows, headed, solved)
    piece_rows = rows_dev // col_count
    my_piece = solved[:piece_rows]
    for j in range(1, col_count):
        perm = [(k * col_count, k * col_count + j) for k in range(row_count)]
        got = lax.ppermute(solved[j * piece_rows:(j + 1) * piece_rows], ("row", "col"), perm)
        my_piece = jnp.where(col_id == j, got, my_piece)

    ratio = row_count // col_count
    perm = []
    for k in range(row_count):
        c, b = divmod(k, ratio)
        for j in range(col_count):
            perm.append((k * col_count + j, (col_count * b + j) * col_count + c))
    mine = lax.ppermute(my_piece, ("row", "col"), perm)
    column_panel = lax.all_gather(mine, "row", axis=0, tiled=True)
    shifted = [my_piece]
    for s_ in range(1, col_count):
        perm = [
            (k * col_count + j, k * col_count + (j + s_) % col_count)
            for k in range(row_count)
            for j in range(col_count)
        ]
        shifted.append(lax.ppermute(my_piece, ("row", "col"), perm))
    turned = jnp.stack([shifted[(col_count - m) % col_count] for m in range(col_count)] * 2)
    panel_here = lax.dynamic_slice_in_dim(turned, (col_count - col_id) % col_count, col_count, 0)
    panel_here = panel_here.reshape(rows_dev, PANEL)
    update = lax.dot_general(
        panel_here,
        column_panel,
        (((1,), (1,)), ((), ())),
        precision=lax.Precision.HIGH,
        preferred_element_type=jnp.float32,
    )
    global_rows = row_id * rows_dev + jnp.arange(rows_dev, dtype=jnp.int32)
    global_cols = col_id * cols_dev + jnp.arange(cols_dev, dtype=jnp.int32)
    trailing = (global_rows[:, None] >= PANEL) & (global_cols[None, :] >= PANEL)
    factored = (front + delta) - jnp.where(trailing, update, 0.0)
    return (factored, panel_here)


def solution(mesh):
    in_specs = (
        P("row", "col"),
        P(("row", "col"), None, None),
        P(("row", "col"), None),
        P(("row", "col")),
    )
    out_specs = (P("row", "col"), P("row", None))
    return jax.shard_map(shards, mesh=mesh, in_specs=in_specs, out_specs=out_specs, check_vma=False)
```
